512 devices in a mesh: wa: 32 (over x, y, core), ha: 16 (over z).
Axes of the slice: x: 4, y: 4, z: 16, core: 2. Of those that a mesh axis runs over, the one named last changes fastest.
Arguments:
- residual_in: bfloat16 [192, 16384], P('ha', 'wa'), may hold values from -43.25 to 43.25
- grad_out: bfloat16 [192, 16384], P('ha', 'wa'), may hold values from -6 to 6
- norm_gain: bfloat16 [16384], P('wa'), may hold values from 0.099609375 to 1.8984375
- w_gate: bfloat16 [16384, 26624], P('wa', 'ha'), may hold values from -0.0390625 to 0.0390625
- w_up: bfloat16 [16384, 26624], P('wa', 'ha'), may hold values from -0.0390625 to 0.0390625
- w_down: bfloat16 [26624, 16384], P('ha', 'wa'), may hold values from -0.030643146 to 0.030643146
Outputs:
- grad_in: bfloat16 [192, 16384], P('ha', 'wa')
The draws below stay inside these ranges and needn't reach their ends.
All inputs are finite; a program needn't handle non-finite values.
Results may differ from the reference program's by a relative error of at most 0.0053.
Values may be sent and summed in bfloat16 or wider, within the bound.
No kernel may reach another device: no remote copies, remote signals or barrier semaphores. Data moves between devices by JAX's collectives and lax.ppermute only.
A program may use at most 64 MiB of HBM per device.

```python
import jax
import jax.numpy as jnp
from jax import lax

D = 16384
FF = 26624
TOKENS = 192


def draw_residual_in(key, part):
    key_rows, key_cols, key_base = jax.random.split(key, 3)
    row_scale = jnp.exp(jax.random.uniform(key_rows, (TOKENS, 1), jnp.float32) * jnp.log(10.0))
    col_rand = jnp.exp(jax.random.uniform(key_cols, (1, D), jnp.float32) * jnp.log(10.0))
    ramp = jnp.arange(D, dtype=jnp.float32)[None, :] / (D - 1)
    col_scale = col_rand * (1.0 + 0.8 * ramp)
    base = jnp.clip(jax.random.normal(key_base, (TOKENS, D), jnp.float32), -4.0, 4.0)
    return (0.06 * base * row_scale * col_scale).astype(jnp.bfloat16)


def draw_w_gate(key, part):
    shared_key = jax.random.fold_in(key, 101)
    shared = jax.random.normal(shared_key, (D, FF), jnp.float32)
    return (jnp.clip(shared, -5.0, 5.0) * D ** (-0.5)).astype(jnp.bfloat16)


def draw_w_up(key, part):
    shared_key = jax.random.fold_in(key, 101)
    own_key = jax.random.fold_in(key, 102)
    shared = jax.random.normal(shared_key, (D, FF), jnp.float32)
    own = jax.random.normal(own_key, (D, FF), jnp.float32)
    mixed = 0.7 * shared + 0.714 * own
    return (jnp.clip(mixed, -5.0, 5.0) * D ** (-0.5)).astype(jnp.bfloat16)


def draw_w_down(key, part):
    own_key = jax.random.fold_in(key, 201)
    row_key = jax.random.fold_in(key, 202)
    own = jax.random.normal(own_key, (FF, D), jnp.float32)
    common_row = jax.random.normal(row_key, (1, D), jnp.float32)
    mixed = own + 0.6 * common_row
    return (jnp.clip(mixed, -5.0, 5.0) * FF ** (-0.5)).astype(jnp.bfloat16)


def levels(key, dims, cuts, low, high):
    loudness, own = 1.0, jax.random.fold_in(key, 6)
    for dim, shards_of in cuts:
        draws = jnp.exp(jax.random.uniform(jax.random.fold_in(own, dim), (shards_of,), jnp.float32, low / len(cuts), high / len(cuts)))
        loudness = loudness * jnp.repeat(draws, dims[dim] // shards_of).reshape([-1 if axis == dim else 1 for axis in range(len(dims))])
    return loudness


def noise(key, extent, spread, limit, cuts=(), kind=jnp.bfloat16):
    drawn = spread * jax.random.normal(key, extent, jnp.float32)
    if cuts:
        drawn = drawn * levels(key, extent, cuts, -0.22, 0.18)
    return jnp.clip(drawn, -limit, limit).astype(kind)


def setup_inputs(seed: int = 0) -> dict:
    key_list = jax.random.split(jax.random.key(seed), 7)
    return {
        "residual_in": draw_residual_in(jax.random.fold_in(key_list[6], 71), 0),
        "grad_out": noise(key_list[1], (TOKENS, D), 1.0, 6.0, ((0, 16), (1, 32))),
        "norm_gain": jnp.clip(1.0 + 0.18 * jax.random.normal(key_list[2], (D,), jnp.float32), 0.099609375, 1.8984375).astype(jnp.bfloat16),
        "w_gate": draw_w_gate(jax.random.fold_in(key_list[6], 71), 0),
        "w_up": draw_w_up(jax.random.fold_in(key_list[6], 71), 0),
        "w_down": draw_w_down(jax.random.fold_in(key_list[6], 71), 0),
    }


def reference(residual_in, grad_out, norm_gain, w_gate, w_up, w_down):
    stream = residual_in.astype(jnp.float32)
    inv_rms = lax.rsqrt(lax.optimization_barrier(jnp.mean(stream * stream, axis=1, keepdims=True)) + 1e-05)
    gain_f = norm_gain.astype(jnp.float32)
    normed = (stream * inv_rms * gain_f).astype(jnp.bfloat16)
    gate = jnp.dot(normed, w_gate, preferred_element_type=jnp.float32)
    up = jnp.dot(normed, w_up, preferred_element_type=jnp.float32)
    d_hidden = jnp.dot(grad_out, w_down.T, preferred_element_type=jnp.float32)
    sig = jax.nn.sigmoid(gate)
    d_up = (d_hidden * gate * sig).astype(jnp.bfloat16)
    d_gate = (d_hidden * up * sig * (1.0 + gate * (1.0 - sig))).astype(jnp.bfloat16)
    d_normed = jnp.dot(d_gate, w_gate.T, preferred_element_type=jnp.float32)
    d_normed = d_normed + jnp.dot(d_up, w_up.T, preferred_element_type=jnp.float32)
    scaled = d_normed * gain_f
    row_dot = lax.optimization_barrier(jnp.sum(scaled * stream, axis=1, keepdims=True))
    grad_in = grad_out.astype(jnp.float32) + inv_rms * scaled - stream * inv_rms ** 3 * row_dot / D
    return grad_in.astype(jnp.bfloat16)
```

```python
import jax
import jax.numpy as jnp
from jax import lax
from jax.sharding import PartitionSpec as P

D = 16384
EXTRA = 128


def gate_grads(gate, up, d_hidden):
    sig = jax.nn.sigmoid(gate)
    d_up = (d_hidden * gate * sig).astype(jnp.bfloat16)
    d_gate = (d_hidden * up * sig * (1.0 + gate * (1.0 - sig))).astype(jnp.bfloat16)
    return d_gate, d_up


def local(residual_in, grad_out, norm_gain, w_gate, w_up, w_down):
    n_ha = lax.axis_size("ha")
    rows = residual_in.shape[0]
    ff = w_gate.shape[1]
    gain_f = norm_gain.astype(jnp.float32)

    piece = lax.all_gather(jnp.stack([residual_in, grad_out]), "ha", axis=1, tiled=True)
    stream_all = piece[0].astype(jnp.float32)
    sq_part = jnp.sum(stream_all * stream_all, axis=1)
    scaled_in = (stream_all * gain_f).astype(jnp.bfloat16)

    gate_part = jnp.dot(scaled_in, w_gate, preferred_element_type=jnp.float32)
    up_part = jnp.dot(scaled_in, w_up, preferred_element_type=jnp.float32)
    back_part = lax.dot_general(
        piece[1], w_down, (((1,), (1,)), ((), ())), preferred_element_type=jnp.float32
    )
    sq_cols = jnp.broadcast_to(sq_part[:, None], (sq_part.shape[0], EXTRA))
    summed = lax.psum(jnp.concatenate([gate_part, up_part, back_part, sq_cols], axis=1), "wa")
    gate_raw = summed[:, :ff]
    up_raw = summed[:, ff : 2 * ff]
    d_hidden = summed[:, 2 * ff : 3 * ff]
    inv_rms_all = lax.rsqrt(summed[:, 3 * ff] / D + 1e-05)[:, None]

    d_gate, d_up = gate_grads(inv_rms_all * gate_raw, inv_rms_all * up_raw, d_hidden)
    dot_part = jnp.sum(
        d_gate.astype(jnp.float32) * gate_raw + d_up.astype(jnp.float32) * up_raw, axis=1
    )
    total = lax.dot_general(
        d_gate, w_gate, (((1,), (1,)), ((), ())), preferred_element_type=jnp.float32
    ) + lax.dot_general(
        d_up, w_up, (((1,), (1,)), ((), ())), preferred_element_type=jnp.float32
    )
    dot_cols = jnp.broadcast_to(dot_part[:, None], (dot_part.shape[0], EXTRA))
    packed = jnp.concatenate([total, dot_cols], axis=1)
    packed = packed.reshape(n_ha, rows, packed.shape[1])
    mine = lax.psum_scatter(packed, "ha", scatter_dimension=0, tiled=True)[0]
    d_normed = mine[:, : total.shape[1]]
    row_dot = mine[:, total.shape[1]][:, None]

    start = lax.axis_index("ha") * rows
    inv_rms = lax.dynamic_slice_in_dim(inv_rms_all, start, rows, axis=0)
    stream = residual_in.astype(jnp.float32)
    scaled = d_normed * gain_f
    grad_in = grad_out.astype(jnp.float32) + inv_rms * scaled - stream * inv_rms**3 * row_dot / D
    return grad_in.astype(jnp.bfloat16)


def solution(mesh):
    placed = (P("ha", "wa"), P("ha", "wa"), P("wa"), P("wa", "ha"), P("wa", "ha"), P("ha", "wa"))
    return jax.shard_map(
        local, mesh=mesh, in_specs=placed, out_specs=P("ha", "wa"), check_vma=False
    )
```

```python
import jax
import jax.numpy as jnp
from jax import lax
from jax.sharding import Mesh
from jax.sharding import PartitionSpec as P

D = 16384
WA = ("x", "y", "core")


def gate_grads(gate, up, d_hidden):
    sig = jax.nn.sigmoid(gate)
    d_up = (d_hidden * gate * sig).astype(jnp.bfloat16)
    d_gate = (d_hidden * up * sig * (1.0 + gate * (1.0 - sig))).astype(jnp.bfloat16)
    return d_gate, d_up


def local(residual_in, grad_out, norm_gain, w_gate, w_up, w_down):
    rows = residual_in.shape[0]
    gain_f = norm_gain.astype(jnp.float32)

    piece = lax.all_gather(jnp.stack([residual_in, grad_out]), "ha", axis=1, tiled=True)
    stream_all = piece[0].astype(jnp.float32)
    squares = jnp.sum(stream_all * stream_all, axis=1)
    squares = lax.psum(lax.psum(lax.psum(squares, "core"), "y"), "x")
    inv_rms_all = lax.rsqrt(squares / D + 1e-05)[:, None]
    normed = (stream_all * inv_rms_all * gain_f).astype(jnp.bfloat16)

    gate_part = jnp.dot(normed, w_gate, preferred_element_type=jnp.float32)
    up_part = jnp.dot(normed, w_up, preferred_element_type=jnp.float32)
    back_part = lax.dot_general(
        piece[1], w_down, (((1,), (1,)), ((), ())), preferred_element_type=jnp.float32
    )
    summed = lax.psum(jnp.stack([gate_part, up_part, back_part]), WA)
    gate, up, d_hidden = summed[0], summed[1], summed[2]

    d_gate, d_up = gate_grads(gate, up, d_hidden)
    dot_part = jnp.sum(d_gate.astype(jnp.float32) * gate + d_up.astype(jnp.float32) * up, axis=1)
    total = lax.dot_general(
        d_gate, w_gate, (((1,), (1,)), ((), ())), preferred_element_type=jnp.float32
    ) + lax.dot_general(
        d_up, w_up, (((1,), (1,)), ((), ())), preferred_element_type=jnp.float32
    )
    n_ha, width = lax.axis_size("ha"), total.shape[1]
    dot_rows = jnp.pad(dot_part.reshape(n_ha, 1, rows), ((0, 0), (0, 0), (0, width - rows)))
    packed = jnp.concatenate([total.reshape(n_ha, rows, width), dot_rows], axis=1)
    mine = lax.psum_scatter(packed.reshape(-1, width), "ha", scatter_dimension=0, tiled=True)
    d_normed = mine[:rows]

    start = lax.axis_index("ha") * rows
    inv_rms = lax.dynamic_slice_in_dim(inv_rms_all, start, rows, axis=0)
    row_dot = mine[rows, :rows][:, None] / inv_rms
    stream = residual_in.astype(jnp.float32)
    scaled = d_normed * gain_f
    grad_in = grad_out.astype(jnp.float32) + inv_rms * scaled - stream * inv_rms**3 * row_dot / D
    return grad_in.astype(jnp.bfloat16)


def solution(mesh):
    devices = mesh.devices if mesh.axis_names[0] == "wa" else mesh.devices.T
    view = Mesh(devices.reshape(4, 4, 2, devices.shape[1]), WA + ("ha",))
    placed = (P("ha", WA), P("ha", WA), P(WA), P(WA, "ha"), P(WA, "ha"), P("ha", WA))
    return jax.shard_map(
        local, mesh=view, in_specs=placed, out_specs=P("ha", WA), check_vma=False
    )
```

```python
import jax
import jax.numpy as jnp
from jax import lax
from jax.sharding import Mesh
from jax.sharding import PartitionSpec as P

D = 16384
WA = ("x", "y", "core")


def gate_grads(gate, up, d_hidden):
    sig = jax.nn.sigmoid(gate)
    d_up = (d_hidden * gate * sig).astype(jnp.bfloat16)
    d_gate = (d_hidden * up * sig * (1.0 + gate * (1.0 - sig))).astype(jnp.bfloat16)
    return d_gate, d_up


def _partner(axis, bit):
    n = lax.axis_size(axis)
    return [(i, i ^ (1 << bit)) for i in range(n)]


def _bit(axis, bit):
    return (lax.axis_index(axis) >> bit) & 1


def gather_rows(x, axis):
    n = lax.axis_size(axis)
    held = x[:, None]
    for bit in reversed(range(n.bit_length() - 1)):
        got = lax.ppermute(held, axis, _partner(axis, bit))
        low = _bit(axis, bit) == 0
        held = jnp.stack([jnp.where(low, held, got), jnp.where(low, got, held)], axis=2)
        held = held.reshape(held.shape[0], -1, *held.shape[3:])
    return held.reshape(x.shape[0], n * x.shape[1], x.shape[2])


def scatter_sum(x, axis):
    n = lax.axis_size(axis)
    for bit in range(n.bit_length() - 1):
        pairs = x.reshape(-1, 2, *x.shape[1:])
        mine = _bit(axis, bit)
        keep = lax.dynamic_index_in_dim(pairs, mine, axis=1, keepdims=False)
        send = lax.dynamic_index_in_dim(pairs, 1 - mine, axis=1, keepdims=False)
        x = keep + lax.ppermute(send, axis, _partner(axis, bit))
    return x[0]


def local(residual_in, grad_out, norm_gain, w_gate, w_up, w_down):
    rows = residual_in.shape[0]
    gain_f = norm_gain.astype(jnp.float32)

    piece = gather_rows(jnp.stack([residual_in, grad_out]), "ha")
    stream_all = piece[0].astype(jnp.float32)
    squares = jnp.sum(stream_all * stream_all, axis=1)
    squares = lax.psum(lax.psum(lax.psum(squares, "core"), "y"), "x")
    inv_rms_all = lax.rsqrt(squares / D + 1e-05)[:, None]
    normed = (stream_all * inv_rms_all * gain_f).astype(jnp.bfloat16)

    gate_part = jnp.dot(normed, w_gate, preferred_element_type=jnp.float32)
    up_part = jnp.dot(normed, w_up, preferred_element_type=jnp.float32)
    back_part = lax.dot_general(
        piece[1], w_down, (((1,), (1,)), ((), ())), preferred_element_type=jnp.float32
    )
    summed = lax.psum(jnp.stack([gate_part, up_part, back_part]), WA)
    gate, up, d_hidden = summed[0], summed[1], summed[2]

    d_gate, d_up = gate_grads(gate, up, d_hidden)
    dot_part = jnp.sum(d_gate.astype(jnp.float32) * gate + d_up.astype(jnp.float32) * up, axis=1)
    total = lax.dot_general(
        d_gate, w_gate, (((1,), (1,)), ((), ())), preferred_element_type=jnp.float32
    ) + lax.dot_general(
        d_up, w_up, (((1,), (1,)), ((), ())), preferred_element_type=jnp.float32
    )
    n_ha, width = lax.axis_size("ha"), total.shape[1]
    dot_rows = jnp.pad(dot_part.reshape(n_ha, 1, rows), ((0, 0), (0, 0), (0, width - rows)))
    packed = jnp.concatenate([total.reshape(n_ha, rows, width), dot_rows], axis=1)
    mine = scatter_sum(packed, "ha")
    d_normed = mine[:rows]

    start = lax.axis_index("ha") * rows
    inv_rms = lax.dynamic_slice_in_dim(inv_rms_all, start, rows, axis=0)
    row_dot = mine[rows, :rows][:, None] / inv_rms
    stream = residual_in.astype(jnp.float32)
    scaled = d_normed * gain_f
    grad_in = grad_out.astype(jnp.float32) + inv_rms * scaled - stream * inv_rms**3 * row_dot / D
    return grad_in.astype(jnp.bfloat16)


def solution(mesh):
    devices = mesh.devices if mesh.axis_names[0] == "wa" else mesh.devices.T
    view = Mesh(devices.reshape(4, 4, 2, devices.shape[1]), WA + ("ha",))
    placed = (P("ha", WA), P("ha", WA), P(WA), P(WA, "ha"), P(WA, "ha"), P("ha", WA))
    return jax.shard_map(
        local, mesh=view, in_specs=placed, out_specs=P("ha", WA), check_vma=False
    )
```

```python
import jax
import jax.numpy as jnp
from jax import lax
from jax.sharding import Mesh
from jax.sharding import PartitionSpec as P

D = 16384
WA = ("x", "y", "core")


def gate_grads(gate, up, d_hidden):
    sig = jax.nn.sigmoid(gate)
    d_up = (d_hidden * gate * sig).astype(jnp.bfloat16)
    d_gate = (d_hidden * up * sig * (1.0 + gate * (1.0 - sig))).astype(jnp.bfloat16)
    return d_gate, d_up


def _partner(axis, bit):
    n = lax.axis_size(axis)
    return [(i, i ^ (1 << bit)) for i in range(n)]


def _bit(axis, bit):
    return (lax.axis_index(axis) >> bit) & 1


def gather_rows(x, axis):
    n = lax.axis_size(axis)
    held = x[:, None]
    for bit in reversed(range(n.bit_length() - 1)):
        got = lax.ppermute(held, axis, _partner(axis, bit))
        low = _bit(axis, bit) == 0
        held = jnp.stack([jnp.where(low, held, got), jnp.where(low, got, held)], axis=2)
        held = held.reshape(held.shape[0], -1, *held.shape[3:])
    return held.reshape(x.shape[0], n * x.shape[1], x.shape[2])


def scatter_sum(x, axis):
    n = lax.axis_size(axis)
    for bit in range(n.bit_length() - 1):
        pairs = x.reshape(-1, 2, *x.shape[1:])
        mine = _bit(axis, bit)
        keep = lax.dynamic_index_in_dim(pairs, mine, axis=1, keepdims=False)
        send = lax.dynamic_index_in_dim(pairs, 1 - mine, axis=1, keepdims=False)
        x = keep + lax.ppermute(send, axis, _partner(axis, bit))
    return x[0]


def local(residual_in, grad_out, norm_gain, w_gate, w_up, w_down):
    rows = residual_in.shape[0]
    gain_f = norm_gain.astype(jnp.float32)

    piece = lax.all_gather(jnp.stack([residual_in, grad_out]), "ha", axis=1, tiled=True)
    stream_all = piece[0].astype(jnp.float32)
    squares = jnp.sum(stream_all * stream_all, axis=1)
    squares = lax.psum(lax.psum(lax.psum(squares, "core"), "y"), "x")
    inv_rms_all = lax.rsqrt(squares / D + 1e-05)[:, None]
    normed = (stream_all * inv_rms_all * gain_f).astype(jnp.bfloat16)

    gate_part = jnp.dot(normed, w_gate, preferred_element_type=jnp.float32)
    up_part = jnp.dot(normed, w_up, preferred_element_type=jnp.float32)
    back_part = lax.dot_general(
        piece[1], w_down, (((1,), (1,)), ((), ())), preferred_element_type=jnp.float32
    )
    partial = jnp.stack([gate_part, up_part, back_part])
    half = lax.psum_scatter(partial, "core", scatter_dimension=1, tiled=True)
    half = lax.psum(half, ("x", "y"))
    gate, up, d_hidden = half[0], half[1], half[2]

    d_gate, d_up = gate_grads(gate, up, d_hidden)
    dot_half = jnp.sum(d_gate.astype(jnp.float32) * gate + d_up.astype(jnp.float32) * up, axis=1)
    grads = lax.all_gather(jnp.stack([d_gate, d_up]), "core", axis=1, tiled=True)
    d_gate, d_up = grads[0], grads[1]
    dot_part = lax.all_gather(dot_half, "core", axis=0, tiled=True)
    total = lax.dot_general(
        d_gate, w_gate, (((1,), (1,)), ((), ())), preferred_element_type=jnp.float32
    ) + lax.dot_general(
        d_up, w_up, (((1,), (1,)), ((), ())), preferred_element_type=jnp.float32
    )
    n_ha, width = lax.axis_size("ha"), total.shape[1]
    dot_rows = jnp.pad(dot_part.reshape(n_ha, 1, rows), ((0, 0), (0, 0), (0, width - rows)))
    packed = jnp.concatenate([total.reshape(n_ha, rows, width), dot_rows], axis=1)
    mine = scatter_sum(packed, "ha")
    d_normed = mine[:rows]

    start = lax.axis_index("ha") * rows
    inv_rms = lax.dynamic_slice_in_dim(inv_rms_all, start, rows, axis=0)
    row_dot = mine[rows, :rows][:, None] / inv_rms
    stream = residual_in.astype(jnp.float32)
    scaled = d_normed * gain_f
    grad_in = grad_out.astype(jnp.float32) + inv_rms * scaled - stream * inv_rms**3 * row_dot / D
    return grad_in.astype(jnp.bfloat16)


def solution(mesh):
    devices = mesh.devices if mesh.axis_names[0] == "wa" else mesh.devices.T
    view = Mesh(devices.reshape(4, 4, 2, devices.shape[1]), WA + ("ha",))
    placed = (P("ha", WA), P("ha", WA), P(WA), P(WA, "ha"), P(WA, "ha"), P("ha", WA))
    return jax.shard_map(
        local, mesh=view, in_specs=placed, out_specs=P("ha", WA), check_vma=False
    )
```

```python
import jax
import jax.numpy as jnp
from jax import lax
from jax.sharding import Mesh
from jax.sharding import PartitionSpec as P

D = 16384
WA = ("x", "y", "core")


def gate_grads(gate, up, d_hidden):
    sig = jax.nn.sigmoid(gate)
    d_up = (d_hidden * gate * sig).astype(jnp.bfloat16)
    d_gate = (d_hidden * up * sig * (1.0 + gate * (1.0 - sig))).astype(jnp.bfloat16)
    return d_gate, d_up


def scatter_sum(x, axis):
    n = lax.axis_size(axis)
    for shift in range(0, n.bit_length() - 1, 2):
        groups = x.reshape(-1, 4, *x.shape[1:])
        mine = (lax.axis_index(axis) >> shift) & 3
        total = lax.dynamic_index_in_dim(groups, mine, axis=1, keepdims=False)
        for k in (1, 2, 3):
            send = lax.dynamic_index_in_dim(groups, mine ^ k, axis=1, keepdims=False)
            total = total + lax.ppermute(send, axis, [(i, i ^ (k << shift)) for i in range(n)])
        x = total
    return x[0]


def local(residual_in, grad_out, norm_gain, w_gate, w_up, w_down):
    rows = residual_in.shape[0]
    gain_f = norm_gain.astype(jnp.float32)

    piece = lax.all_gather(jnp.stack([residual_in, grad_out]), "ha", axis=1, tiled=True)
    stream_all = piece[0].astype(jnp.float32)
    squares = jnp.sum(stream_all * stream_all, axis=1)
    squares = lax.psum(lax.psum(lax.psum(squares, "core"), "y"), "x")
    inv_rms_all = lax.rsqrt(squares / D + 1e-05)[:, None]
    normed = (stream_all * inv_rms_all * gain_f).astype(jnp.bfloat16)

    gate_part = jnp.dot(normed, w_gate, preferred_element_type=jnp.float32)
    up_part = jnp.dot(normed, w_up, preferred_element_type=jnp.float32)
    back_part = lax.dot_general(
        piece[1], w_down, (((1,), (1,)), ((), ())), preferred_element_type=jnp.float32
    )
    summed = lax.psum(jnp.stack([gate_part, up_part, back_part]), WA)
    gate, up, d_hidden = summed[0], summed[1], summed[2]

    d_gate, d_up = gate_grads(gate, up, d_hidden)
    dot_part = jnp.sum(d_gate.astype(jnp.float32) * gate + d_up.astype(jnp.float32) * up, axis=1)
    total = lax.dot_general(
        d_gate, w_gate, (((1,), (1,)), ((), ())), preferred_element_type=jnp.float32
    ) + lax.dot_general(
        d_up, w_up, (((1,), (1,)), ((), ())), preferred_element_type=jnp.float32
    )
    n_ha, width = lax.axis_size("ha"), total.shape[1]
    dot_rows = jnp.pad(dot_part.reshape(n_ha, 1, rows), ((0, 0), (0, 0), (0, width - rows)))
    packed = jnp.concatenate([total.reshape(n_ha, rows, width), dot_rows], axis=1)
    mine = scatter_sum(packed, "ha")
    d_normed = mine[:rows]

    start = lax.axis_index("ha") * rows
    inv_rms = lax.dynamic_slice_in_dim(inv_rms_all, start, rows, axis=0)
    row_dot = mine[rows, :rows][:, None] / inv_rms
    stream = residual_in.astype(jnp.float32)
    scaled = d_normed * gain_f
    grad_in = grad_out.astype(jnp.float32) + inv_rms * scaled - stream * inv_rms**3 * row_dot / D
    return grad_in.astype(jnp.bfloat16)


def solution(mesh):
    devices = mesh.devices if mesh.axis_names[0] == "wa" else mesh.devices.T
    view = Mesh(devices.reshape(4, 4, 2, devices.shape[1]), WA + ("ha",))
    placed = (P("ha", WA), P("ha", WA), P(WA), P(WA, "ha"), P(WA, "ha"), P("ha", WA))
    return jax.shard_map(
        local, mesh=view, in_specs=placed, out_specs=P("ha", WA), check_vma=False
    )
```

```python
import jax
import jax.numpy as jnp
from jax import lax
from jax.sharding import Mesh
from jax.sharding import PartitionSpec as P

D = 16384
WA = ("x", "y", "core")


def gate_grads(gate, up, d_hidden):
    sig = jax.nn.sigmoid(gate)
    d_up = (d_hidden * gate * sig).astype(jnp.bfloat16)
    d_gate = (d_hidden * up * sig * (1.0 + gate * (1.0 - sig))).astype(jnp.bfloat16)
    return d_gate, d_up


def scatter_sum(x, axis):
    n = lax.axis_size(axis)
    for shift in range(0, n.bit_length() - 1, 2):
        groups = x.reshape(-1, 4, *x.shape[1:])
        mine = (lax.axis_index(axis) >> shift) & 3
        total = lax.dynamic_index_in_dim(groups, mine, axis=1, keepdims=False)
        for k in (1, 2, 3):
            send = lax.dynamic_index_in_dim(groups, mine ^ k, axis=1, keepdims=False)
            total = total + lax.ppermute(send, axis, [(i, i ^ (k << shift)) for i in range(n)])
        x = total
    return x[0]


def _exchange(axis, k):
    return [(i, i ^ k) for i in range(lax.axis_size(axis))]


def scatter_blocks(x, axes):
    for axis in axes:
        g = lax.axis_size(axis)
        groups = x.reshape(x.shape[0], -1, g, *x.shape[2:])
        mine = lax.axis_index(axis)
        total = lax.dynamic_index_in_dim(groups, mine, axis=2, keepdims=False)
        for k in range(1, g):
            send = lax.dynamic_index_in_dim(groups, mine ^ k, axis=2, keepdims=False)
            total = total + lax.ppermute(send, axis, _exchange(axis, k))
        x = total
    return x


def gather_blocks(x, axes):
    for axis in reversed(axes):
        g = lax.axis_size(axis)
        mine = lax.axis_index(axis)
        held = [x] + [lax.ppermute(x, axis, _exchange(axis, k)) for k in range(1, g)]
        placed = []
        for d in range(g):
            pick = held[g - 1]
            for k in reversed(range(g - 1)):
                pick = jnp.where((mine ^ d) == k, held[k], pick)
            placed.append(pick)
        x = jnp.stack(placed, axis=2).reshape(x.shape[0], -1, *x.shape[2:])
    return x


def local(residual_in, grad_out, norm_gain, w_gate, w_up, w_down):
    rows = residual_in.shape[0]
    gain_f = norm_gain.astype(jnp.float32)

    piece = lax.all_gather(jnp.stack([residual_in, grad_out]), "ha", axis=1, tiled=True)
    stream_all = piece[0].astype(jnp.float32)
    squares = jnp.sum(stream_all * stream_all, axis=1)
    squares = lax.psum(lax.psum(lax.psum(squares, "core"), "y"), "x")
    inv_rms_all = lax.rsqrt(squares / D + 1e-05)[:, None]
    normed = (stream_all * inv_rms_all * gain_f).astype(jnp.bfloat16)

    gate_part = jnp.dot(normed, w_gate, preferred_element_type=jnp.float32)
    up_part = jnp.dot(normed, w_up, preferred_element_type=jnp.float32)
    back_part = lax.dot_general(
        piece[1], w_down, (((1,), (1,)), ((), ())), preferred_element_type=jnp.float32
    )
    n_wa, width = lax.axis_size(WA), gate_part.shape[1]
    partial = jnp.stack([gate_part, up_part, back_part]).reshape(3, n_wa, -1, width)
    part = scatter_blocks(partial, WA[::-1])[:, 0]
    gate, up, d_hidden = part[0], part[1], part[2]
    d_gate, d_up = gate_grads(gate, up, d_hidden)
    dot_rows = jnp.sum(d_gate.astype(jnp.float32) * gate + d_up.astype(jnp.float32) * up, axis=1)
    dot_hi = dot_rows.astype(jnp.bfloat16)
    dot_lo = (dot_rows - dot_hi.astype(jnp.float32)).astype(jnp.bfloat16)
    extra = jnp.zeros_like(d_gate).at[:, 0].set(dot_hi).at[:, 1].set(dot_lo)
    grads = gather_blocks(jnp.stack([d_gate, d_up, extra])[:, None], WA[::-1])
    grads = grads.reshape(3, -1, width)
    d_gate, d_up = grads[0], grads[1]
    dot_part = grads[2][:, 0].astype(jnp.float32) + grads[2][:, 1].astype(jnp.float32)
    total = lax.dot_general(
        d_gate, w_gate, (((1,), (1,)), ((), ())), preferred_element_type=jnp.float32
    ) + lax.dot_general(
        d_up, w_up, (((1,), (1,)), ((), ())), preferred_element_type=jnp.float32
    )
    n_ha, width = lax.axis_size("ha"), total.shape[1]
    dot_rows = jnp.pad(dot_part.reshape(n_ha, 1, rows), ((0, 0), (0, 0), (0, width - rows)))
    packed = jnp.concatenate([total.reshape(n_ha, rows, width), dot_rows], axis=1)
    mine = scatter_sum(packed, "ha")
    d_normed = mine[:rows]

    start = lax.axis_index("ha") * rows
    inv_rms = lax.dynamic_slice_in_dim(inv_rms_all, start, rows, axis=0)
    row_dot = mine[rows, :rows][:, None] / inv_rms
    stream = residual_in.astype(jnp.float32)
    scaled = d_normed * gain_f
    grad_in = grad_out.astype(jnp.float32) + inv_rms * scaled - stream * inv_rms**3 * row_dot / D
    return grad_in.astype(jnp.bfloat16)


def solution(mesh):
    devices = mesh.devices if mesh.axis_names[0] == "wa" else mesh.devices.T
    view = Mesh(devices.reshape(4, 4, 2, devices.shape[1]), WA + ("ha",))
    placed = (P("ha", WA), P("ha", WA), P(WA), P(WA, "ha"), P(WA, "ha"), P("ha", WA))
    return jax.shard_map(
        local, mesh=view, in_specs=placed, out_specs=P("ha", WA), check_vma=False
    )
```

```python
import jax
import jax.numpy as jnp
from jax import lax
from jax.sharding import Mesh
from jax.sharding import PartitionSpec as P

D = 16384
WA = ("x", "y", "core")


def gate_grads(gate, up, d_hidden):
    sig = jax.nn.sigmoid(gate)
    d_up = (d_hidden * gate * sig).astype(jnp.bfloat16)
    d_gate = (d_hidden * up * sig * (1.0 + gate * (1.0 - sig))).astype(jnp.bfloat16)
    return d_gate, d_up


def scatter_sum(x, axis):
    n = lax.axis_size(axis)
    for shift in range(0, n.bit_length() - 1, 2):
        groups = x.reshape(-1, 4, *x.shape[1:])
        mine = (lax.axis_index(axis) >> shift) & 3
        total = lax.dynamic_index_in_dim(groups, mine, axis=1, keepdims=False)
        for k in (1, 2, 3):
            send = lax.dynamic_index_in_dim(groups, mine ^ k, axis=1, keepdims=False)
            total = total + lax.ppermute(send, axis, [(i, i ^ (k << shift)) for i in range(n)])
        x = total
    return x[0]


def _exchange(axis, k):
    return [(i, i ^ k) for i in range(lax.axis_size(axis))]


def scatter_blocks(x, axes):
    for axis in axes:
        g = lax.axis_size(axis)
        groups = x.reshape(x.shape[0], -1, g, *x.shape[2:])
        mine = lax.axis_index(axis)
        total = lax.dynamic_index_in_dim(groups, mine, axis=2, keepdims=False)
        for k in range(1, g):
            send = lax.dynamic_index_in_dim(groups, mine ^ k, axis=2, keepdims=False)
            total = total + lax.ppermute(send, axis, _exchange(axis, k))
        x = total
    return x


def gather_blocks(x, axes):
    for axis in reversed(axes):
        g = lax.axis_size(axis)
        mine = lax.axis_index(axis)
        held = [x] + [lax.ppermute(x, axis, _exchange(axis, k)) for k in range(1, g)]
        placed = []
        for d in range(g):
            pick = held[g - 1]
            for k in reversed(range(g - 1)):
                pick = jnp.where((mine ^ d) == k, held[k], pick)
            placed.append(pick)
        x = jnp.stack(placed, axis=2).reshape(x.shape[0], -1, *x.shape[2:])
    return x


def local(residual_in, grad_out, norm_gain, w_gate, w_up, w_down):
    rows = residual_in.shape[0]
    gain_f = norm_gain.astype(jnp.float32)

    piece = lax.all_gather(jnp.stack([residual_in, grad_out]), "ha", axis=1, tiled=True)
    stream_all = piece[0].astype(jnp.float32)
    squares = jnp.sum(stream_all * stream_all, axis=1)
    squares = lax.psum(lax.psum(lax.psum(squares, "core"), "y"), "x")
    inv_rms_all = lax.rsqrt(squares / D + 1e-05)[:, None]
    normed = (stream_all * inv_rms_all * gain_f).astype(jnp.bfloat16)

    gate_part = jnp.dot(normed, w_gate, preferred_element_type=jnp.float32)
    up_part = jnp.dot(normed, w_up, preferred_element_type=jnp.float32)
    back_part = lax.dot_general(
        piece[1], w_down, (((1,), (1,)), ((), ())), preferred_element_type=jnp.float32
    )
    n_wa, width = lax.axis_size(WA), gate_part.shape[1]
    partial = jnp.stack([gate_part, up_part, back_part]).reshape(3, n_wa, -1)
    partial = partial.transpose(1, 0, 2).reshape(1, n_wa, -1)
    part = scatter_blocks(partial, WA[::-1]).reshape(3, -1, width)
    gate, up, d_hidden = part[0], part[1], part[2]
    d_gate, d_up = gate_grads(gate, up, d_hidden)
    dot_rows = jnp.sum(d_gate.astype(jnp.float32) * gate + d_up.astype(jnp.float32) * up, axis=1)
    dot_hi = dot_rows.astype(jnp.bfloat16)
    dot_lo = (dot_rows - dot_hi.astype(jnp.float32)).astype(jnp.bfloat16)
    extra = jnp.zeros_like(d_gate).at[:, 0].set(dot_hi).at[:, 1].set(dot_lo)
    grads = gather_blocks(jnp.stack([d_gate, d_up, extra]).reshape(1, 1, -1), WA[::-1])
    grads = grads.reshape(n_wa, 3, -1, width).transpose(1, 0, 2, 3).reshape(3, -1, width)
    d_gate, d_up = grads[0], grads[1]
    dot_part = grads[2][:, 0].astype(jnp.float32) + grads[2][:, 1].astype(jnp.float32)
    total = lax.dot_general(
        d_gate, w_gate, (((1,), (1,)), ((), ())), preferred_element_type=jnp.float32
    ) + lax.dot_general(
        d_up, w_up, (((1,), (1,)), ((), ())), preferred_element_type=jnp.float32
    )
    n_ha, width = lax.axis_size("ha"), total.shape[1]
    dot_rows = jnp.pad(dot_part.reshape(n_ha, 1, rows), ((0, 0), (0, 0), (0, width - rows)))
    packed = jnp.concatenate([total.reshape(n_ha, rows, width), dot_rows], axis=1)
    mine = scatter_sum(packed, "ha")
    d_normed = mine[:rows]

    start = lax.axis_index("ha") * rows
    inv_rms = lax.dynamic_slice_in_dim(inv_rms_all, start, rows, axis=0)
    row_dot = mine[rows, :rows][:, None] / inv_rms
    stream = residual_in.astype(jnp.float32)
    scaled = d_normed * gain_f
    grad_in = grad_out.astype(jnp.float32) + inv_rms * scaled - stream * inv_rms**3 * row_dot / D
    return grad_in.astype(jnp.bfloat16)


def solution(mesh):
    devices = mesh.devices if mesh.axis_names[0] == "wa" else mesh.devices.T
    view = Mesh(devices.reshape(4, 4, 2, devices.shape[1]), WA + ("ha",))
    placed = (P("ha", WA), P("ha", WA), P(WA), P(WA, "ha"), P(WA, "ha"), P("ha", WA))
    return jax.shard_map(
        local, mesh=view, in_specs=placed, out_specs=P("ha", WA), check_vma=False
    )
```

```python
import jax
import jax.numpy as jnp
from jax import lax
from jax.sharding import Mesh
from jax.sharding import PartitionSpec as P

D = 16384
WA = ("x", "y", "core")


def gate_grads(gate, up, d_hidden):
    sig = jax.nn.sigmoid(gate)
    d_up = (d_hidden * gate * sig).astype(jnp.bfloat16)
    d_gate = (d_hidden * up * sig * (1.0 + gate * (1.0 - sig))).astype(jnp.bfloat16)
    return d_gate, d_up


def scatter_sum(x, axis):
    n = lax.axis_size(axis)
    for shift in range(0, n.bit_length() - 1, 2):
        groups = x.reshape(-1, 4, *x.shape[1:])
        mine = (lax.axis_index(axis) >> shift) & 3
        total = lax.dynamic_index_in_dim(groups, mine, axis=1, keepdims=False)
        for k in (1, 2, 3):
            send = lax.dynamic_index_in_dim(groups, mine ^ k, axis=1, keepdims=False)
            total = total + lax.ppermute(send, axis, [(i, i ^ (k << shift)) for i in range(n)])
        x = total
    return x[0]


def local(residual_in, grad_out, norm_gain, w_gate, w_up, w_down):
    rows = residual_in.shape[0]
    gain_f = norm_gain.astype(jnp.float32)

    piece = lax.all_gather(jnp.stack([residual_in, grad_out]), "ha", axis=1, tiled=True)
    stream_all = piece[0].astype(jnp.float32)
    squares = jnp.sum(stream_all * stream_all, axis=1)
    squares = lax.psum(lax.psum(lax.psum(squares, "core"), "y"), "x")
    inv_rms_all = lax.rsqrt(squares / D + 1e-05)[:, None]
    normed = (stream_all * inv_rms_all * gain_f).astype(jnp.bfloat16)

    gate_part = jnp.dot(normed, w_gate, preferred_element_type=jnp.float32)
    up_part = jnp.dot(normed, w_up, preferred_element_type=jnp.float32)
    back_part = lax.dot_general(
        piece[1], w_down, (((1,), (1,)), ((), ())), preferred_element_type=jnp.float32
    )
    n_wa, width = lax.axis_size(WA), gate_part.shape[1]
    partial = jnp.stack([gate_part, up_part, back_part]).reshape(3, n_wa, -1)
    partial = partial.transpose(1, 0, 2).reshape(n_wa, -1, 128)
    part = lax.psum_scatter(partial, WA, scatter_dimension=0, tiled=True).reshape(3, -1, width)
    gate, up, d_hidden = part[0], part[1], part[2]
    d_gate, d_up = gate_grads(gate, up, d_hidden)
    dot_rows = jnp.sum(d_gate.astype(jnp.float32) * gate + d_up.astype(jnp.float32) * up, axis=1)
    dot_hi = dot_rows.astype(jnp.bfloat16)
    dot_lo = (dot_rows - dot_hi.astype(jnp.float32)).astype(jnp.bfloat16)
    extra = jnp.zeros_like(d_gate).at[:, 0].set(dot_hi).at[:, 1].set(dot_lo)
    grads = lax.all_gather(jnp.stack([d_gate, d_up, extra]).reshape(1, -1, 128), WA, axis=0, tiled=True)
    grads = grads.reshape(n_wa, 3, -1, width).transpose(1, 0, 2, 3).reshape(3, -1, width)
    d_gate, d_up = grads[0], grads[1]
    dot_part = grads[2][:, 0].astype(jnp.float32) + grads[2][:, 1].astype(jnp.float32)
    total = lax.dot_general(
        d_gate, w_gate, (((1,), (1,)), ((), ())), preferred_element_type=jnp.float32
    ) + lax.dot_general(
        d_up, w_up, (((1,), (1,)), ((), ())), preferred_element_type=jnp.float32
    )
    n_ha, width = lax.axis_size("ha"), total.shape[1]
    dot_rows = jnp.pad(dot_part.reshape(n_ha, 1, rows), ((0, 0), (0, 0), (0, width - rows)))
    packed = jnp.concatenate([total.reshape(n_ha, rows, width), dot_rows], axis=1)
    mine = scatter_sum(packed, "ha")
    d_normed = mine[:rows]

    start = lax.axis_index("ha") * rows
    inv_rms = lax.dynamic_slice_in_dim(inv_rms_all, start, rows, axis=0)
    row_dot = mine[rows, :rows][:, None] / inv_rms
    stream = residual_in.astype(jnp.float32)
    scaled = d_normed * gain_f
    grad_in = grad_out.astype(jnp.float32) + inv_rms * scaled - stream * inv_rms**3 * row_dot / D
    return grad_in.astype(jnp.bfloat16)


def solution(mesh):
    devices = mesh.devices if mesh.axis_names[0] == "wa" else mesh.devices.T
    view = Mesh(devices.reshape(4, 4, 2, devices.shape[1]), WA + ("ha",))
    placed = (P("ha", WA), P("ha", WA), P(WA), P(WA, "ha"), P(WA, "ha"), P("ha", WA))
    return jax.shard_map(
        local, mesh=view, in_specs=placed, out_specs=P("ha", WA), check_vma=False
    )
```

```python
import jax
import jax.numpy as jnp
from jax import lax
from jax.sharding import Mesh
from jax.sharding import PartitionSpec as P

D = 16384
WA = ("x", "y", "core")


def gate_grads(gate, up, d_hidden):
    sig = jax.nn.sigmoid(gate)
    d_up = (d_hidden * gate * sig).astype(jnp.bfloat16)
    d_gate = (d_hidden * up * sig * (1.0 + gate * (1.0 - sig))).astype(jnp.bfloat16)
    return d_gate, d_up


def scatter_sum(x, axis):
    n = lax.axis_size(axis)
    for shift in range(0, n.bit_length() - 1, 2):
        groups = x.reshape(-1, 4, *x.shape[1:])
        mine = (lax.axis_index(axis) >> shift) & 3
        total = lax.dynamic_index_in_dim(groups, mine, axis=1, keepdims=False)
        for k in (1, 2, 3):
            send = lax.dynamic_index_in_dim(groups, mine ^ k, axis=1, keepdims=False)
            total = total + lax.ppermute(send, axis, [(i, i ^ (k << shift)) for i in range(n)])
        x = total
    return x[0]


def gather_rows(x, axis):
    n = lax.axis_size(axis)
    held = x[:, None]
    for shift in reversed(range(0, n.bit_length() - 1, 2)):
        mine = (lax.axis_index(axis) >> shift) & 3
        got = [held] + [lax.ppermute(held, axis, [(i, i ^ (k << shift)) for i in range(n)]) for k in (1, 2, 3)]
        placed = []
        for d in range(4):
            pick = got[3]
            for k in (2, 1, 0):
                pick = jnp.where((mine ^ d) == k, got[k], pick)
            placed.append(pick)
        held = jnp.stack(placed, axis=2).reshape(x.shape[0], -1, *x.shape[1:])
    return held.reshape(x.shape[0], n * x.shape[1], x.shape[2])


def local(residual_in, grad_out, norm_gain, w_gate, w_up, w_down):
    rows = residual_in.shape[0]
    gain_f = norm_gain.astype(jnp.float32)

    piece = gather_rows(jnp.stack([residual_in, grad_out]), "ha")
    stream_all = piece[0].astype(jnp.float32)
    squares = jnp.sum(stream_all * stream_all, axis=1)
    squares = lax.psum(lax.psum(lax.psum(squares, "core"), "y"), "x")
    inv_rms_all = lax.rsqrt(squares / D + 1e-05)[:, None]
    normed = (stream_all * inv_rms_all * gain_f).astype(jnp.bfloat16)

    gate_part = jnp.dot(normed, w_gate, preferred_element_type=jnp.float32)
    up_part = jnp.dot(normed, w_up, preferred_element_type=jnp.float32)
    back_part = lax.dot_general(
        piece[1], w_down, (((1,), (1,)), ((), ())), preferred_element_type=jnp.float32
    )
    summed = lax.psum(jnp.stack([gate_part, up_part, back_part]), WA)
    gate, up, d_hidden = summed[0], summed[1], summed[2]

    d_gate, d_up = gate_grads(gate, up, d_hidden)
    dot_part = jnp.sum(d_gate.astype(jnp.float32) * gate + d_up.astype(jnp.float32) * up, axis=1)
    total = lax.dot_general(
        d_gate, w_gate, (((1,), (1,)), ((), ())), preferred_element_type=jnp.float32
    ) + lax.dot_general(
        d_up, w_up, (((1,), (1,)), ((), ())), preferred_element_type=jnp.float32
    )
    n_ha, width = lax.axis_size("ha"), total.shape[1]
    dot_rows = jnp.pad(dot_part.reshape(n_ha, 1, rows), ((0, 0), (0, 0), (0, width - rows)))
    packed = jnp.concatenate([total.reshape(n_ha, rows, width), dot_rows], axis=1)
    mine = scatter_sum(packed, "ha")
    d_normed = mine[:rows]

    start = lax.axis_index("ha") * rows
    inv_rms = lax.dynamic_slice_in_dim(inv_rms_all, start, rows, axis=0)
    row_dot = mine[rows, :rows][:, None] / inv_rms
    stream = residual_in.astype(jnp.float32)
    scaled = d_normed * gain_f
    grad_in = grad_out.astype(jnp.float32) + inv_rms * scaled - stream * inv_rms**3 * row_dot / D
    return grad_in.astype(jnp.bfloat16)


def solution(mesh):
    devices = mesh.devices if mesh.axis_names[0] == "wa" else mesh.devices.T
    view = Mesh(devices.reshape(4, 4, 2, devices.shape[1]), WA + ("ha",))
    placed = (P("ha", WA), P("ha", WA), P(WA), P(WA, "ha"), P(WA, "ha"), P("ha", WA))
    return jax.shard_map(
        local, mesh=view, in_specs=placed, out_specs=P("ha", WA), check_vma=False
    )
```
